512 devices in a mesh: dp: 64 (over z, y), tensor: 8 (over x, core).
Axes of the slice: x: 4, y: 8, z: 8, core: 2. Of those that a mesh axis runs over, the one named last changes fastest.
Arguments:
- hidden: bfloat16 [192, 256, 14336], P('dp', None, 'tensor'), may hold values from -6 to 6
- out_grad: bfloat16 [192, 256, 4096], P('dp', None, 'tensor'), may hold values from -0.29882812 to 0.29882812
- proj_in: bfloat16 [64, 14336], P(None, 'tensor'), may hold values from -0.046875 to 0.046875
- proj_out: bfloat16 [64, 4096], P(None, 'tensor'), may hold values from -0.09375 to 0.09375
- left_inv: float32 [64, 64], replicated, may hold values from -0.15 to 3, as said below
- right_inv: float32 [64, 64], replicated, may hold values from -0.15 to 3, as said below
- lengths: int32 [192], P('dp'), may hold values from 64 to 256
- language: int32 [192], P('dp'), may hold values from 0 to 99
- owner: int32 [100], replicated, may hold values from 0 to 63, as said below
Outputs:
- seq_grads: float32 [192, 4096], P('dp', 'tensor')
- owned_means: float32 [128, 4096], P('dp', 'tensor')
The draws below stay inside these ranges and needn't reach their ends.
Inputs may be any that keep to these rules, and one draw needn't show every extreme that they name: `left_inv`: symmetric; diagonal entries 1 or more, off-diagonal entries of magnitude 0.15 or less. `right_inv`: symmetric; diagonal entries 1 or more, off-diagonal entries of magnitude 0.15 or less. Every owner holds 1 or 2 languages, and some owner holds 2.
All inputs are finite; a program needn't handle non-finite values.
Results may differ from the reference program's by a relative error of at most 0.0003.
Values sent between devices are 32-bit elements; how exact they have to be, the bound alone decides.
No kernel may reach another device: no remote copies, remote signals or barrier semaphores. Data moves between devices by JAX's collectives and lax.ppermute only.
A program may use at most 64 MiB of HBM per device.

```python
import math
import jax
import jax.numpy as jnp
import numpy as np
from jax import lax

D = 4096
FF = 14336
R = 64
LANGS = 100
SEQ_LEN = 256
SEQS = 192
OWNERS = 64
SLOTS = 2
OWNED = 128


def inverse_factor(key):
    off_key, diag_key = jax.random.split(key)
    spread = 0.1
    lower_end = 1.0
    upper_end = 2.0
    off_part = jax.random.uniform(off_key, (R, R), jnp.float32, -spread, spread)
    off_part = 0.5 * (off_part + off_part.T)
    diagonal = jax.random.uniform(diag_key, (R,), jnp.float32, lower_end, upper_end)
    identity = jnp.eye(R, dtype=jnp.float32)
    return off_part * (1.0 - identity) + identity * diagonal[None, :]


def draw_left_inv(key, part):
    return inverse_factor(jax.random.fold_in(key, 11))


def draw_right_inv(key, part):
    return inverse_factor(jax.random.fold_in(key, 23))


def draw_owner(key, part):
    order = jax.random.permutation(jax.random.fold_in(key, 37), LANGS)
    return (order % OWNERS).astype(jnp.int32)


def place_ends(drawn, rng, smallest, largest):
    longest = drawn.shape.index(max(drawn.shape))
    spots = []
    for shift in (0, 1):
        where = [jax.random.randint(jax.random.fold_in(rng, axis), (), 0, length) for axis, length in enumerate(drawn.shape)]
        where[longest] = (where[longest] + shift) % drawn.shape[longest]
        spots.append(tuple(where))
    return drawn.at[spots[0]].set(smallest).at[spots[1]].set(largest)


def shard_levels(rng, dims, cuts, least, largest):
    level, own = 1.0, jax.random.fold_in(rng, 6)
    for position, parts in cuts:
        heights = jnp.exp(jax.random.uniform(jax.random.fold_in(own, position), (parts,), jnp.float32, least / len(cuts), largest / len(cuts)))
        level = level * jnp.repeat(heights, dims[position] // parts).reshape([-1 if axis == position else 1 for axis in range(len(dims))])
    return level


def cumulative_ranks(count, lean):
    weights = [(1 << 20) // math.isqrt(standing ** lean) + 1 for standing in range(1, count + 1)]
    deviation = 1 + sum(weights) // (1 << 30)
    return np.cumsum(np.array([max(1, weight // deviation) for weight in weights]))


def skewed_ids(key, extent, number_of, lean):
    grid = cumulative_ranks(number_of, lean)
    ticket = jax.random.randint(jax.random.fold_in(key, 1), extent, 0, int(grid[number_of - 1]))
    standing = jnp.searchsorted(jnp.asarray(grid, jnp.int32), ticket, side="right")
    return jax.random.permutation(jax.random.fold_in(key, 2), number_of)[standing].astype(jnp.int32)


def scatter_about(own_key, extent, scale, limit, pieces=(), kind=jnp.bfloat16):
    values = scale * jax.random.normal(own_key, extent, jnp.float32)
    if pieces:
        values = values * shard_levels(own_key, extent, pieces, -0.22, 0.18)
    return jnp.clip(values, -limit, limit).astype(kind)


def setup_inputs(seed: int = 0) -> dict:
    streams_of = jax.random.split(jax.random.key(seed), 10)
    return {
        "hidden": scatter_about(streams_of[0], (SEQS, SEQ_LEN, FF), 1.0, 6.0, ((0, 64), (2, 8))),
        "out_grad": scatter_about(streams_of[1], (SEQS, SEQ_LEN, D), 0.05, 0.29882812, ((0, 64), (2, 8))),
        "proj_in": scatter_about(streams_of[2], (R, FF), FF ** -0.5, 0.046875, ((1, 8),)),
        "proj_out": scatter_about(streams_of[3], (R, D), D ** -0.5, 0.09375, ((1, 8),)),
        "left_inv": draw_left_inv(jax.random.fold_in(streams_of[9], 71), 0),
        "right_inv": draw_right_inv(jax.random.fold_in(streams_of[9], 71), 0),
        "lengths": place_ends(jax.random.randint(streams_of[6], (SEQS,), SEQ_LEN // 4, SEQ_LEN + 1), jax.random.fold_in(streams_of[6], 1), SEQ_LEN // 4, SEQ_LEN).astype(jnp.int32),
        "language": place_ends(skewed_ids(streams_of[7], (SEQS,), LANGS, 2), jax.random.fold_in(streams_of[7], 3), 0, LANGS - 1).astype(jnp.int32),
        "owner": draw_owner(jax.random.fold_in(streams_of[9], 71), 0),
    }


def project(values, projection):
    flattened = values.reshape(-1, values.shape[-1])
    return lax.dot_general(flattened, projection, (((1,), (1,)), ((), ())), preferred_element_type=jnp.float32)


def reference(hidden, out_grad, proj_in, proj_out, left_inv, right_inv, lengths, language, owner):
    highest = lax.Precision.HIGHEST
    left_full = project(hidden, proj_in).reshape(SEQS, SEQ_LEN, R)
    right_full = project(out_grad, proj_out).reshape(SEQS, SEQ_LEN, R)
    token_mask = (jnp.arange(SEQ_LEN, dtype=jnp.int32)[None, :] < lengths[:, None]).astype(jnp.float32)
    right_full = right_full * token_mask[:, :, None]
    seq_grads = jnp.einsum("sti,stj->sij", left_full, right_full, precision=highest)
    left_done = jnp.einsum("ik,skj->sij", left_inv, seq_grads, precision=highest)
    preconditioned = jnp.einsum("sik,kj->sij", left_done, right_inv, precision=highest)
    lang_index = jnp.arange(LANGS, dtype=jnp.int32)
    lang_hot = (language[:, None] == lang_index[None, :]).astype(jnp.float32)
    lang_count = jnp.sum(lang_hot, axis=0)
    lang_total_sum = jnp.dot(lang_hot.T, preconditioned.reshape(SEQS, R * R), precision=highest)
    lang_mean = lang_total_sum / jnp.maximum(lang_count, 1.0)[:, None]
    same_owner = (owner[:, None] == owner[None, :]) & (lang_index[None, :] < lang_index[:, None])
    lang_slot = jnp.sum(same_owner.astype(jnp.int32), axis=1)
    lang_place = owner * SLOTS + lang_slot
    place_hot = (lang_place[:, None] == jnp.arange(OWNED, dtype=jnp.int32)[None, :]).astype(jnp.float32)
    owned_means = jnp.dot(place_hot.T, lang_mean, precision=highest)
    return seq_grads.reshape(SEQS, R * R), owned_means
```

```python
import jax
import jax.numpy as jnp
from jax import lax
from jax.sharding import PartitionSpec as P


def project_t(values, projection):
    flattened = values.reshape(-1, values.shape[-1])
    return lax.dot_general(
        projection, flattened, (((1,), (1,)), ((), ())), preferred_element_type=jnp.float32
    )


def tensor_sum(parts, tensor_size):
    feat, tokens = parts.shape
    block = feat // tensor_size
    chunks = parts.reshape(tensor_size, block, tokens)
    mine = jnp.sum(lax.all_to_all(chunks, "tensor", 0, 0, tiled=True), axis=0)
    spread = jnp.broadcast_to(mine[None], (tensor_size, block, tokens))
    whole = lax.all_to_all(spread, "tensor", 0, 0, tiled=True)
    return whole.reshape(feat, tokens)


def per_device(hidden, out_grad, proj_in, proj_out, left_inv, right_inv, lengths, language, owner):
    highest = lax.Precision.HIGHEST
    seq_count = hidden.shape[0]
    seq_length = hidden.shape[1]
    proj_rank = proj_in.shape[0]
    tensor_size = lax.axis_size("tensor")
    row_width = proj_rank // tensor_size
    row_start = lax.axis_index("tensor") * row_width
    left_part = project_t(hidden, proj_in)
    right_part = project_t(out_grad, proj_out)
    both = tensor_sum(jnp.concatenate([left_part, right_part], axis=0), tensor_size)
    left_t = both[:proj_rank].reshape(proj_rank, seq_count, seq_length)
    right_t = both[proj_rank:].reshape(proj_rank, seq_count, seq_length)
    token_mask = (jnp.arange(seq_length, dtype=jnp.int32)[None, :] < lengths[:, None]).astype(
        jnp.float32
    )
    right_t = right_t * token_mask[None, :, :]
    full_grads = jnp.einsum("ist,jst->sij", left_t, right_t, precision=highest)
    inv_rows = lax.dynamic_slice_in_dim(left_inv, row_start, row_width, 0)
    grad_rows = lax.dynamic_slice_in_dim(full_grads, row_start, row_width, 1)
    left_done = jnp.einsum("ik,skj->sij", inv_rows, full_grads, precision=highest)
    pre_rows = jnp.einsum("sik,kj->sij", left_done, right_inv, precision=highest)
    grad_flat = grad_rows.reshape(seq_count, row_width * proj_rank)
    pre_flat = pre_rows.reshape(seq_count, row_width * proj_rank)
    lang_total = owner.shape[0]
    dp_size = lax.axis_size("dp")
    slot_count = (lang_total + dp_size - 1) // dp_size
    owned_rows = slot_count * dp_size
    lang_index = jnp.arange(lang_total, dtype=jnp.int32)
    same_owner = (owner[:, None] == owner[None, :]) & (lang_index[None, :] < lang_index[:, None])
    lang_slot = jnp.sum(same_owner.astype(jnp.int32), axis=1)
    lang_place = owner * slot_count + lang_slot
    lang_hot = (language[:, None] == lang_index[None, :]).astype(jnp.int32)
    seq_place = jnp.sum(lang_hot * lang_place[None, :], axis=1)
    place_hot = (seq_place[:, None] == jnp.arange(owned_rows, dtype=jnp.int32)[None, :]).astype(
        jnp.float32
    )
    slot_table = jnp.dot(place_hot.T, pre_flat, precision=highest)
    slot_counts = jnp.sum(place_hot, axis=0)
    width = slot_table.shape[1]
    count_row = jnp.zeros((dp_size, 1, width), jnp.float32)
    count_row = count_row.at[:, 0, :slot_count].set(slot_counts.reshape(dp_size, slot_count))
    payload = jnp.concatenate(
        [slot_table.reshape(dp_size, slot_count, width), count_row], axis=1
    )
    gathered = jnp.sum(lax.all_to_all(payload, "dp", 0, 0, tiled=True), axis=0)
    summed = gathered[:slot_count]
    counted = gathered[slot_count, :slot_count]
    owned_means = summed / jnp.maximum(counted, 1.0)[:, None]
    return (grad_flat, owned_means)


def solution(mesh):
    return jax.shard_map(
        per_device,
        mesh=mesh,
        in_specs=(
            P("dp", None, "tensor"),
            P("dp", None, "tensor"),
            P(None, "tensor"),
            P(None, "tensor"),
            P(),
            P(),
            P("dp"),
            P("dp"),
            P(),
        ),
        out_specs=(P("dp", "tensor"), P("dp", "tensor")),
        check_vma=False,
    )
```

```python
import jax
import jax.numpy as jnp
from jax import lax
from jax.sharding import PartitionSpec as P


def project_t(values, projection):
    flattened = values.reshape(-1, values.shape[-1])
    return lax.dot_general(
        projection, flattened, (((1,), (1,)), ((), ())), preferred_element_type=jnp.float32
    )


def tensor_sum(parts, tensor_size):
    feat, tokens = parts.shape
    block = feat // tensor_size
    chunks = parts.reshape(tensor_size, block, tokens)
    mine = jnp.sum(lax.all_to_all(chunks, "tensor", 0, 0, tiled=True), axis=0)
    spread = jnp.broadcast_to(mine[None], (tensor_size, block, tokens))
    whole = lax.all_to_all(spread, "tensor", 0, 0, tiled=True)
    return whole.reshape(feat, tokens)


def per_device(hidden, out_grad, proj_in, proj_out, left_inv, right_inv, lengths, language, owner):
    highest = lax.Precision.HIGHEST
    seq_count = hidden.shape[0]
    seq_length = hidden.shape[1]
    proj_rank = proj_in.shape[0]
    tensor_size = lax.axis_size("tensor")
    row_width = proj_rank // tensor_size
    row_start = lax.axis_index("tensor") * row_width
    left_part = project_t(hidden, proj_in)
    right_part = project_t(out_grad, proj_out)
    both = tensor_sum(jnp.concatenate([left_part, right_part], axis=0), tensor_size)
    left_t = both[:proj_rank]
    right_t = both[proj_rank:]
    token_seq = jnp.repeat(lengths, seq_length, total_repeat_length=seq_count * seq_length)
    token_pos = jnp.arange(seq_count * seq_length, dtype=jnp.int32) % seq_length
    right_t = right_t * (token_pos < token_seq).astype(jnp.float32)[None, :]
    full_grads = jnp.stack(
        [
            lax.dot_general(
                left_t[:, s * seq_length : (s + 1) * seq_length],
                right_t[:, s * seq_length : (s + 1) * seq_length],
                (((1,), (1,)), ((), ())),
                precision=highest,
            )
            for s in range(seq_count)
        ]
    )
    inv_rows = lax.dynamic_slice_in_dim(left_inv, row_start, row_width, 0)
    grad_rows = lax.dynamic_slice_in_dim(full_grads, row_start, row_width, 1)
    left_done = jnp.einsum("ik,skj->sij", inv_rows, full_grads, precision=highest)
    pre_rows = jnp.einsum("sik,kj->sij", left_done, right_inv, precision=highest)
    grad_flat = grad_rows.reshape(seq_count, row_width * proj_rank)
    pre_flat = pre_rows.reshape(seq_count, row_width * proj_rank)
    lang_total = owner.shape[0]
    dp_size = lax.axis_size("dp")
    slot_count = (lang_total + dp_size - 1) // dp_size
    owned_rows = slot_count * dp_size
    lang_index = jnp.arange(lang_total, dtype=jnp.int32)
    same_owner = (owner[:, None] == owner[None, :]) & (lang_index[None, :] < lang_index[:, None])
    lang_slot = jnp.sum(same_owner.astype(jnp.int32), axis=1)
    lang_place = owner * slot_count + lang_slot
    lang_hot = (language[:, None] == lang_index[None, :]).astype(jnp.int32)
    seq_place = jnp.sum(lang_hot * lang_place[None, :], axis=1)
    place_hot = (seq_place[:, None] == jnp.arange(owned_rows, dtype=jnp.int32)[None, :]).astype(
        jnp.float32
    )
    slot_table = jnp.dot(place_hot.T, pre_flat, precision=highest)
    slot_counts = jnp.sum(place_hot, axis=0)
    width = slot_table.shape[1]
    count_pad = 128
    payload = jnp.concatenate(
        [
            slot_table.reshape(dp_size, slot_count * width),
            jnp.pad(slot_counts.reshape(dp_size, slot_count), ((0, 0), (0, count_pad - slot_count))),
        ],
        axis=1,
    )
    gathered = jnp.sum(lax.all_to_all(payload, "dp", 0, 0, tiled=True), axis=0)
    summed = gathered[: slot_count * width].reshape(slot_count, width)
    counted = gathered[slot_count * width : slot_count * width + slot_count]
    owned_means = summed / jnp.maximum(counted, 1.0)[:, None]
    return (grad_flat, owned_means)


def solution(mesh):
    return jax.shard_map(
        per_device,
        mesh=mesh,
        in_specs=(
            P("dp", None, "tensor"),
            P("dp", None, "tensor"),
            P(None, "tensor"),
            P(None, "tensor"),
            P(),
            P(),
            P("dp"),
            P("dp"),
            P(),
        ),
        out_specs=(P("dp", "tensor"), P("dp", "tensor")),
        check_vma=False,
    )
```

```python
import jax
import jax.numpy as jnp
from jax import lax
from jax.sharding import PartitionSpec as P


def project(values, projection):
    flattened = values.reshape(-1, values.shape[-1])
    return lax.dot_general(
        flattened, projection, (((1,), (1,)), ((), ())), preferred_element_type=jnp.float32
    )


def tensor_sum(parts, tensor_size):
    tokens, feat = parts.shape
    block = tokens // tensor_size
    chunks = parts.reshape(tensor_size, block, feat)
    mine = jnp.sum(lax.all_to_all(chunks, "tensor", 0, 0, tiled=True), axis=0)
    spread = jnp.broadcast_to(mine[None], (tensor_size, block, feat))
    whole = lax.all_to_all(spread, "tensor", 0, 0, tiled=True)
    return whole.reshape(tokens, feat)


def per_device(hidden, out_grad, proj_in, proj_out, left_inv, right_inv, lengths, language, owner):
    highest = lax.Precision.HIGHEST
    seq_count = hidden.shape[0]
    seq_length = hidden.shape[1]
    proj_rank = proj_in.shape[0]
    tensor_size = lax.axis_size("tensor")
    row_width = proj_rank // tensor_size
    row_start = lax.axis_index("tensor") * row_width
    token_mask = (jnp.arange(seq_length, dtype=jnp.int32)[None, :] < lengths[:, None]).astype(
        jnp.float32
    )
    left_part = project(hidden, proj_in)
    right_part = project(out_grad, proj_out) * token_mask.reshape(-1)[:, None]
    both = tensor_sum(jnp.concatenate([left_part, right_part], axis=1), tensor_size)
    both = both.reshape(seq_count, seq_length, 2 * proj_rank)
    left_full = both[:, :, :proj_rank]
    right_full = both[:, :, proj_rank:]
    full_grads = jnp.einsum("sti,stj->sij", left_full, right_full, precision=highest)
    inv_rows = lax.dynamic_slice_in_dim(left_inv, row_start, row_width, 0)
    grad_rows = lax.dynamic_slice_in_dim(full_grads, row_start, row_width, 1)
    left_done = jnp.einsum("ik,skj->sij", inv_rows, full_grads, precision=highest)
    pre_rows = jnp.einsum("sik,kj->sij", left_done, right_inv, precision=highest)
    grad_flat = grad_rows.reshape(seq_count, row_width * proj_rank)
    pre_flat = pre_rows.reshape(seq_count, row_width * proj_rank)
    lang_total = owner.shape[0]
    dp_size = lax.axis_size("dp")
    slot_count = (lang_total + dp_size - 1) // dp_size
    owned_rows = slot_count * dp_size
    lang_index = jnp.arange(lang_total, dtype=jnp.int32)
    same_owner = (owner[:, None] == owner[None, :]) & (lang_index[None, :] < lang_index[:, None])
    lang_slot = jnp.sum(same_owner.astype(jnp.int32), axis=1)
    lang_place = owner * slot_count + lang_slot
    lang_hot = (language[:, None] == lang_index[None, :]).astype(jnp.int32)
    seq_place = jnp.sum(lang_hot * lang_place[None, :], axis=1)
    place_hot = (seq_place[:, None] == jnp.arange(owned_rows, dtype=jnp.int32)[None, :]).astype(
        jnp.float32
    )
    slot_table = jnp.dot(place_hot.T, pre_flat, precision=highest)
    slot_counts = jnp.sum(place_hot, axis=0)
    width = slot_table.shape[1]
    count_pad = 128
    payload = jnp.concatenate(
        [
            slot_table.reshape(dp_size, 1, slot_count * width),
            jnp.pad(
                slot_counts.reshape(dp_size, 1, slot_count),
                ((0, 0), (0, 0), (0, count_pad - slot_count)),
            ),
        ],
        axis=2,
    )
    gathered = jnp.sum(lax.all_to_all(payload, "dp", 0, 0, tiled=True), axis=(0, 1))
    summed = gathered[: slot_count * width].reshape(slot_count, width)
    counted = gathered[slot_count * width : slot_count * width + slot_count]
    owned_means = summed / jnp.maximum(counted, 1.0)[:, None]
    return (grad_flat, owned_means)


def solution(mesh):
    return jax.shard_map(
        per_device,
        mesh=mesh,
        in_specs=(
            P("dp", None, "tensor"),
            P("dp", None, "tensor"),
            P(None, "tensor"),
            P(None, "tensor"),
            P(),
            P(),
            P("dp"),
            P("dp"),
            P(),
        ),
        out_specs=(P("dp", "tensor"), P("dp", "tensor")),
        check_vma=False,
    )
```

```python
import jax
import jax.numpy as jnp
from jax import lax
from jax.sharding import PartitionSpec as P


def project(values, projection):
    flattened = values.reshape(-1, values.shape[-1])
    return lax.dot_general(
        flattened, projection, (((1,), (1,)), ((), ())), preferred_element_type=jnp.float32
    )


def per_device(hidden, out_grad, proj_in, proj_out, left_inv, right_inv, lengths, language, owner):
    highest = lax.Precision.HIGHEST
    seq_count = hidden.shape[0]
    seq_length = hidden.shape[1]
    proj_rank = proj_in.shape[0]
    tensor_size = lax.axis_size("tensor")
    row_width = proj_rank // tensor_size
    left_part = project(hidden, proj_in)
    right_part = project(out_grad, proj_out)
    parts = jnp.concatenate([left_part, right_part], axis=1)
    tokens = seq_count * seq_length
    block = tokens // tensor_size
    chunks = parts.reshape(tensor_size, block, 2 * proj_rank)
    mine = jnp.sum(lax.all_to_all(chunks, "tensor", 0, 0, tiled=True), axis=0)
    token_at = lax.axis_index("tensor") * block + jnp.arange(block, dtype=jnp.int32)
    token_seq = token_at // seq_length
    token_pos = token_at % seq_length
    seq_index = jnp.arange(seq_count, dtype=jnp.int32)
    weight = (token_seq[None, :] == seq_index[:, None]) & (token_pos[None, :] < lengths[:, None])
    right_seq = mine[None, :, proj_rank:] * weight.astype(jnp.float32)[:, :, None]
    grads_part = jnp.einsum("ti,stj->sij", mine[:, :proj_rank], right_seq, precision=highest)
    left_done = jnp.einsum("ik,skj->sij", left_inv, grads_part, precision=highest)
    pre_part = jnp.einsum("sik,kj->sij", left_done, right_inv, precision=highest)
    stacked = jnp.stack([grads_part, pre_part], axis=1)
    stacked = stacked.reshape(seq_count, 2, tensor_size, row_width, proj_rank)
    stacked = stacked.transpose(2, 0, 1, 3, 4)
    rows = jnp.sum(lax.all_to_all(stacked, "tensor", 0, 0, tiled=True), axis=0)
    grad_flat = rows[:, 0].reshape(seq_count, row_width * proj_rank)
    pre_flat = rows[:, 1].reshape(seq_count, row_width * proj_rank)
    lang_total = owner.shape[0]
    dp_size = lax.axis_size("dp")
    slot_count = (lang_total + dp_size - 1) // dp_size
    owned_rows = slot_count * dp_size
    lang_index = jnp.arange(lang_total, dtype=jnp.int32)
    same_owner = (owner[:, None] == owner[None, :]) & (lang_index[None, :] < lang_index[:, None])
    lang_slot = jnp.sum(same_owner.astype(jnp.int32), axis=1)
    lang_place = owner * slot_count + lang_slot
    lang_hot = (language[:, None] == lang_index[None, :]).astype(jnp.int32)
    seq_place = jnp.sum(lang_hot * lang_place[None, :], axis=1)
    place_hot = (seq_place[:, None] == jnp.arange(owned_rows, dtype=jnp.int32)[None, :]).astype(
        jnp.float32
    )
    slot_table = jnp.dot(place_hot.T, pre_flat, precision=highest)
    slot_counts = jnp.sum(place_hot, axis=0)
    width = slot_table.shape[1]
    count_pad = 128
    payload = jnp.concatenate(
        [
            slot_table.reshape(dp_size, 1, slot_count * width),
            jnp.pad(
                slot_counts.reshape(dp_size, 1, slot_count),
                ((0, 0), (0, 0), (0, count_pad - slot_count)),
            ),
        ],
        axis=2,
    )
    gathered = jnp.sum(lax.all_to_all(payload, "dp", 0, 0, tiled=True), axis=(0, 1))
    summed = gathered[: slot_count * width].reshape(slot_count, width)
    counted = gathered[slot_count * width : slot_count * width + slot_count]
    owned_means = summed / jnp.maximum(counted, 1.0)[:, None]
    return (grad_flat, owned_means)


def solution(mesh):
    return jax.shard_map(
        per_device,
        mesh=mesh,
        in_specs=(
            P("dp", None, "tensor"),
            P("dp", None, "tensor"),
            P(None, "tensor"),
            P(None, "tensor"),
            P(),
            P(),
            P("dp"),
            P("dp"),
            P(),
        ),
        out_specs=(P("dp", "tensor"), P("dp", "tensor")),
        check_vma=False,
    )
```

```python
import jax
import jax.numpy as jnp
from jax import lax
from jax.sharding import PartitionSpec as P


def project(values, projection):
    flattened = values.reshape(-1, values.shape[-1])
    return lax.dot_general(
        flattened, projection, (((1,), (1,)), ((), ())), preferred_element_type=jnp.float32
    )


def per_device(hidden, out_grad, proj_in, proj_out, left_inv, right_inv, lengths, language, owner):
    highest = lax.Precision.HIGHEST
    seq_count = hidden.shape[0]
    seq_length = hidden.shape[1]
    proj_rank = proj_in.shape[0]
    tensor_size = lax.axis_size("tensor")
    row_width = proj_rank // tensor_size
    left_part = project(hidden, proj_in)
    right_part = project(out_grad, proj_out)
    parts = jnp.concatenate([left_part, right_part], axis=1)
    tokens = seq_count * seq_length
    block = tokens // tensor_size
    chunks = parts.reshape(tensor_size, block, 2 * proj_rank)
    mine = jnp.sum(lax.all_to_all(chunks, "tensor", 0, 0, tiled=True), axis=0)
    token_at = lax.axis_index("tensor") * block + jnp.arange(block, dtype=jnp.int32)
    token_seq = token_at // seq_length
    token_pos = token_at % seq_length
    seq_index = jnp.arange(seq_count, dtype=jnp.int32)
    weight = (token_seq[None, :] == seq_index[:, None]) & (token_pos[None, :] < lengths[:, None])
    right_seq = mine[None, :, proj_rank:] * weight.astype(jnp.float32)[:, :, None]
    grads_part = jnp.einsum("ti,stj->sij", mine[:, :proj_rank], right_seq, precision=highest)
    left_done = jnp.einsum("ik,skj->sij", left_inv, grads_part, precision=highest)
    pre_part = jnp.einsum("sik,kj->sij", left_done, right_inv, precision=highest)
    stacked = jnp.concatenate([grads_part, pre_part], axis=2)
    stacked = stacked.reshape(seq_count, tensor_size, row_width, 2 * proj_rank)
    stacked = stacked.transpose(1, 0, 2, 3)
    rows = jnp.sum(lax.all_to_all(stacked, "tensor", 0, 0, tiled=True), axis=0)
    grad_flat = rows[:, :, :proj_rank].reshape(seq_count, row_width * proj_rank)
    pre_flat = rows[:, :, proj_rank:].reshape(seq_count, row_width * proj_rank)
    lang_total = owner.shape[0]
    dp_size = lax.axis_size("dp")
    slot_count = (lang_total + dp_size - 1) // dp_size
    owned_rows = slot_count * dp_size
    lang_index = jnp.arange(lang_total, dtype=jnp.int32)
    same_owner = (owner[:, None] == owner[None, :]) & (lang_index[None, :] < lang_index[:, None])
    lang_slot = jnp.sum(same_owner.astype(jnp.int32), axis=1)
    lang_place = owner * slot_count + lang_slot
    lang_hot = (language[:, None] == lang_index[None, :]).astype(jnp.int32)
    seq_place = jnp.sum(lang_hot * lang_place[None, :], axis=1)
    slot_index = jnp.arange(owned_rows, dtype=jnp.int32).reshape(dp_size, 1, slot_count)
    place_match = seq_place[:, None, None, None] == slot_index[None]
    slot_sums = jnp.sum(
        jnp.where(place_match[..., None], pre_flat[:, None, None, None, :], 0.0), axis=0
    )
    slot_counts = jnp.sum(place_match.astype(jnp.float32), axis=0)
    width = pre_flat.shape[1]
    count_pad = 128
    payload = jnp.concatenate(
        [
            slot_sums.reshape(dp_size, 1, slot_count * width),
            jnp.pad(slot_counts, ((0, 0), (0, 0), (0, count_pad - slot_count))),
        ],
        axis=2,
    )
    gathered = jnp.sum(lax.all_to_all(payload, "dp", 0, 0, tiled=True), axis=(0, 1))
    summed = gathered[: slot_count * width].reshape(slot_count, width)
    counted = gathered[slot_count * width : slot_count * width + slot_count]
    owned_means = summed / jnp.maximum(counted, 1.0)[:, None]
    return (grad_flat, owned_means)


def solution(mesh):
    return jax.shard_map(
        per_device,
        mesh=mesh,
        in_specs=(
            P("dp", None, "tensor"),
            P("dp", None, "tensor"),
            P(None, "tensor"),
            P(None, "tensor"),
            P(),
            P(),
            P("dp"),
            P("dp"),
            P(),
        ),
        out_specs=(P("dp", "tensor"), P("dp", "tensor")),
        check_vma=False,
    )
```

```python
import jax
import jax.numpy as jnp
from jax import lax
from jax.experimental import pallas as pl
from jax.sharding import PartitionSpec as P


def _project_kernel(hidden_ref, grad_ref, proj_in_ref, proj_out_ref, out_ref):
    contract = (((1,), (1,)), ((), ()))
    rank = proj_in_ref.shape[0]
    out_ref[:, :rank] = lax.dot_general(
        hidden_ref[...], proj_in_ref[...], contract, preferred_element_type=jnp.float32
    )
    out_ref[:, rank:] = lax.dot_general(
        grad_ref[...], proj_out_ref[...], contract, preferred_element_type=jnp.float32
    )


def project_both(hidden, out_grad, proj_in, proj_out, tile):
    hidden = hidden.reshape(-1, hidden.shape[-1])
    out_grad = out_grad.reshape(-1, out_grad.shape[-1])
    tokens = hidden.shape[0]
    rank = proj_in.shape[0]
    return pl.pallas_call(
        _project_kernel,
        grid=(tokens // tile,),
        in_specs=[
            pl.BlockSpec((tile, hidden.shape[1]), lambda i: (i, 0)),
            pl.BlockSpec((tile, out_grad.shape[1]), lambda i: (i, 0)),
            pl.BlockSpec(proj_in.shape, lambda i: (0, 0)),
            pl.BlockSpec(proj_out.shape, lambda i: (0, 0)),
        ],
        out_specs=pl.BlockSpec((tile, 2 * rank), lambda i: (i, 0)),
        out_shape=jax.ShapeDtypeStruct((tokens, 2 * rank), jnp.float32),
    )(hidden, out_grad, proj_in, proj_out)


def per_device(hidden, out_grad, proj_in, proj_out, left_inv, right_inv, lengths, language, owner):
    highest = lax.Precision.HIGHEST
    seq_count = hidden.shape[0]
    seq_length = hidden.shape[1]
    proj_rank = proj_in.shape[0]
    tensor_size = lax.axis_size("tensor")
    row_width = proj_rank // tensor_size
    parts = project_both(hidden, out_grad, proj_in, proj_out, seq_length)
    tokens = seq_count * seq_length
    block = tokens // tensor_size
    chunks = parts.reshape(tensor_size, block, 2 * proj_rank)
    mine = jnp.sum(lax.all_to_all(chunks, "tensor", 0, 0, tiled=True), axis=0)
    token_at = lax.axis_index("tensor") * block + jnp.arange(block, dtype=jnp.int32)
    token_seq = token_at // seq_length
    token_pos = token_at % seq_length
    seq_index = jnp.arange(seq_count, dtype=jnp.int32)
    weight = (token_seq[None, :] == seq_index[:, None]) & (token_pos[None, :] < lengths[:, None])
    right_seq = mine[None, :, proj_rank:] * weight.astype(jnp.float32)[:, :, None]
    grads_part = jnp.einsum("ti,stj->sij", mine[:, :proj_rank], right_seq, precision=highest)
    left_done = jnp.einsum("ik,skj->sij", left_inv, grads_part, precision=highest)
    pre_part = jnp.einsum("sik,kj->sij", left_done, right_inv, precision=highest)
    stacked = jnp.concatenate([grads_part, pre_part], axis=2)
    stacked = stacked.reshape(seq_count, tensor_size, row_width, 2 * proj_rank)
    stacked = stacked.transpose(1, 0, 2, 3)
    rows = jnp.sum(lax.all_to_all(stacked, "tensor", 0, 0, tiled=True), axis=0)
    grad_flat = rows[:, :, :proj_rank].reshape(seq_count, row_width * proj_rank)
    pre_flat = rows[:, :, proj_rank:].reshape(seq_count, row_width * proj_rank)
    lang_total = owner.shape[0]
    dp_size = lax.axis_size("dp")
    slot_count = (lang_total + dp_size - 1) // dp_size
    owned_rows = slot_count * dp_size
    lang_index = jnp.arange(lang_total, dtype=jnp.int32)
    same_owner = (owner[:, None] == owner[None, :]) & (lang_index[None, :] < lang_index[:, None])
    lang_slot = jnp.sum(same_owner.astype(jnp.int32), axis=1)
    lang_place = owner * slot_count + lang_slot
    lang_hot = (language[:, None] == lang_index[None, :]).astype(jnp.int32)
    seq_place = jnp.sum(lang_hot * lang_place[None, :], axis=1)
    slot_index = jnp.arange(owned_rows, dtype=jnp.int32).reshape(dp_size, 1, slot_count)
    place_match = seq_place[:, None, None, None] == slot_index[None]
    slot_sums = jnp.sum(
        jnp.where(place_match[..., None], pre_flat[:, None, None, None, :], 0.0), axis=0
    )
    slot_counts = jnp.sum(place_match.astype(jnp.float32), axis=0)
    width = pre_flat.shape[1]
    count_pad = 128
    payload = jnp.concatenate(
        [
            slot_sums.reshape(dp_size, 1, slot_count * width),
            jnp.pad(slot_counts, ((0, 0), (0, 0), (0, count_pad - slot_count))),
        ],
        axis=2,
    )
    gathered = jnp.sum(lax.all_to_all(payload, "dp", 0, 0, tiled=True), axis=(0, 1))
    summed = gathered[: slot_count * width].reshape(slot_count, width)
    counted = gathered[slot_count * width : slot_count * width + slot_count]
    owned_means = summed / jnp.maximum(counted, 1.0)[:, None]
    return (grad_flat, owned_means)


def solution(mesh):
    return jax.shard_map(
        per_device,
        mesh=mesh,
        in_specs=(
            P("dp", None, "tensor"),
            P("dp", None, "tensor"),
            P(None, "tensor"),
            P(None, "tensor"),
            P(),
            P(),
            P("dp"),
            P("dp"),
            P(),
        ),
        out_specs=(P("dp", "tensor"), P("dp", "tensor")),
        check_vma=False,
    )
```

```python
import jax
import jax.numpy as jnp
from jax import lax
from jax.experimental import pallas as pl
from jax.sharding import PartitionSpec as P


def _project_kernel(hidden_ref, grad_ref, proj_in_ref, proj_out_ref, out_ref):
    contract = (((1,), (1,)), ((), ()))
    rank = proj_in_ref.shape[0]
    out_ref[:, :rank] = lax.dot_general(
        hidden_ref[...], proj_in_ref[...], contract, preferred_element_type=jnp.float32
    )
    out_ref[:, rank:] = lax.dot_general(
        grad_ref[...], proj_out_ref[...], contract, preferred_element_type=jnp.float32
    )


def project_both(hidden, out_grad, proj_in, proj_out, tile):
    hidden = hidden.reshape(-1, hidden.shape[-1])
    out_grad = out_grad.reshape(-1, out_grad.shape[-1])
    tokens = hidden.shape[0]
    rank = proj_in.shape[0]
    return pl.pallas_call(
        _project_kernel,
        grid=(tokens // tile,),
        in_specs=[
            pl.BlockSpec((tile, hidden.shape[1]), lambda i: (i, 0)),
            pl.BlockSpec((tile, out_grad.shape[1]), lambda i: (i, 0)),
            pl.BlockSpec(proj_in.shape, lambda i: (0, 0)),
            pl.BlockSpec(proj_out.shape, lambda i: (0, 0)),
        ],
        out_specs=pl.BlockSpec((tile, 2 * rank), lambda i: (i, 0)),
        out_shape=jax.ShapeDtypeStruct((tokens, 2 * rank), jnp.float32),
    )(hidden, out_grad, proj_in, proj_out)


def per_device(hidden, out_grad, proj_in, proj_out, left_inv, right_inv, lengths, language, owner):
    high = lax.Precision.HIGH
    seq_count = hidden.shape[0]
    seq_length = hidden.shape[1]
    proj_rank = proj_in.shape[0]
    tensor_size = lax.axis_size("tensor")
    row_width = proj_rank // tensor_size
    parts = project_both(hidden, out_grad, proj_in, proj_out, seq_length)
    tokens = seq_count * seq_length
    block = tokens // tensor_size
    chunks = parts.reshape(tensor_size, block, 2 * proj_rank)
    mine = jnp.sum(lax.all_to_all(chunks, "tensor", 0, 0, tiled=True), axis=0)
    token_at = lax.axis_index("tensor") * block + jnp.arange(block, dtype=jnp.int32)
    token_seq = token_at // seq_length
    token_pos = token_at % seq_length
    seq_index = jnp.arange(seq_count, dtype=jnp.int32)
    weight = (token_seq[None, :] == seq_index[:, None]) & (token_pos[None, :] < lengths[:, None])
    right_seq = mine[None, :, proj_rank:] * weight.astype(jnp.float32)[:, :, None]
    grads_part = jnp.einsum("ti,stj->sij", mine[:, :proj_rank], right_seq, precision=high)
    left_done = jnp.einsum("ik,skj->sij", left_inv, grads_part, precision=high)
    pre_part = jnp.einsum("sik,kj->sij", left_done, right_inv, precision=high)
    stacked = jnp.concatenate([grads_part, pre_part], axis=2)
    stacked = stacked.reshape(seq_count, tensor_size, row_width, 2 * proj_rank)
    stacked = stacked.transpose(1, 0, 2, 3)
    rows = jnp.sum(lax.all_to_all(stacked, "tensor", 0, 0, tiled=True), axis=0)
    grad_flat = rows[:, :, :proj_rank].reshape(seq_count, row_width * proj_rank)
    pre_flat = rows[:, :, proj_rank:].reshape(seq_count, row_width * proj_rank)
    lang_total = owner.shape[0]
    dp_size = lax.axis_size("dp")
    slot_count = (lang_total + dp_size - 1) // dp_size
    owned_rows = slot_count * dp_size
    lang_index = jnp.arange(lang_total, dtype=jnp.int32)
    same_owner = (owner[:, None] == owner[None, :]) & (lang_index[None, :] < lang_index[:, None])
    lang_slot = jnp.sum(same_owner.astype(jnp.int32), axis=1)
    lang_place = owner * slot_count + lang_slot
    lang_hot = (language[:, None] == lang_index[None, :]).astype(jnp.int32)
    seq_place = jnp.sum(lang_hot * lang_place[None, :], axis=1)
    slot_index = jnp.arange(owned_rows, dtype=jnp.int32).reshape(dp_size, 1, slot_count)
    place_match = seq_place[:, None, None, None] == slot_index[None]
    slot_sums = jnp.sum(
        jnp.where(place_match[..., None], pre_flat[:, None, None, None, :], 0.0), axis=0
    )
    slot_counts = jnp.sum(place_match.astype(jnp.float32), axis=0)
    width = pre_flat.shape[1]
    count_pad = 128
    payload = jnp.concatenate(
        [
            slot_sums.reshape(dp_size, 1, slot_count * width),
            jnp.pad(slot_counts, ((0, 0), (0, 0), (0, count_pad - slot_count))),
        ],
        axis=2,
    )
    gathered = jnp.sum(lax.all_to_all(payload, "dp", 0, 0, tiled=True), axis=(0, 1))
    summed = gathered[: slot_count * width].reshape(slot_count, width)
    counted = gathered[slot_count * width : slot_count * width + slot_count]
    owned_means = summed / jnp.maximum(counted, 1.0)[:, None]
    return (grad_flat, owned_means)


def solution(mesh):
    return jax.shard_map(
        per_device,
        mesh=mesh,
        in_specs=(
            P("dp", None, "tensor"),
            P("dp", None, "tensor"),
            P(None, "tensor"),
            P(None, "tensor"),
            P(),
            P(),
            P("dp"),
            P("dp"),
            P(),
        ),
        out_specs=(P("dp", "tensor"), P("dp", "tensor")),
        check_vma=False,
    )
```

```python
import jax
import jax.numpy as jnp
from jax import lax
from jax.experimental import pallas as pl
from jax.sharding import PartitionSpec as P


def _project_kernel(hidden_ref, grad_ref, proj_in_ref, proj_out_ref, out_ref):
    contract = (((1,), (1,)), ((), ()))
    rank = proj_in_ref.shape[0]
    out_ref[:, :rank] = lax.dot_general(
        hidden_ref[...], proj_in_ref[...], contract, preferred_element_type=jnp.float32
    )
    out_ref[:, rank:] = lax.dot_general(
        grad_ref[...], proj_out_ref[...], contract, preferred_element_type=jnp.float32
    )


def project_both(hidden, out_grad, proj_in, proj_out, tile):
    hidden = hidden.reshape(-1, hidden.shape[-1])
    out_grad = out_grad.reshape(-1, out_grad.shape[-1])
    tokens = hidden.shape[0]
    rank = proj_in.shape[0]
    return pl.pallas_call(
        _project_kernel,
        grid=(tokens // tile,),
        in_specs=[
            pl.BlockSpec((tile, hidden.shape[1]), lambda i: (i, 0)),
            pl.BlockSpec((tile, out_grad.shape[1]), lambda i: (i, 0)),
            pl.BlockSpec(proj_in.shape, lambda i: (0, 0)),
            pl.BlockSpec(proj_out.shape, lambda i: (0, 0)),
        ],
        out_specs=pl.BlockSpec((tile, 2 * rank), lambda i: (i, 0)),
        out_shape=jax.ShapeDtypeStruct((tokens, 2 * rank), jnp.float32),
    )(hidden, out_grad, proj_in, proj_out)


def per_device(hidden, out_grad, proj_in, proj_out, left_inv, right_inv, lengths, language, owner):
    high = lax.Precision.HIGH
    seq_count = hidden.shape[0]
    seq_length = hidden.shape[1]
    proj_rank = proj_in.shape[0]
    tensor_size = lax.axis_size("tensor")
    row_width = proj_rank // tensor_size
    parts = project_both(hidden, out_grad, proj_in, proj_out, seq_length)
    tokens = seq_count * seq_length
    block = tokens // tensor_size
    chunks = parts.reshape(tensor_size, block, 2 * proj_rank)
    mine = jnp.sum(lax.all_to_all(chunks, "tensor", 0, 0, tiled=True), axis=0)
    token_at = lax.axis_index("tensor") * block + jnp.arange(block, dtype=jnp.int32)
    token_seq = token_at // seq_length
    token_pos = token_at % seq_length
    seq_index = jnp.arange(seq_count, dtype=jnp.int32)
    weight = (token_seq[None, :] == seq_index[:, None]) & (token_pos[None, :] < lengths[:, None])
    right_seq = mine[None, :, proj_rank:] * weight.astype(jnp.float32)[:, :, None]
    grads_part = jnp.einsum("ti,stj->sij", mine[:, :proj_rank], right_seq, precision=high)
    left_done = jnp.einsum("ik,skj->sij", left_inv, grads_part, precision=high)
    pre_part = jnp.einsum("sik,kj->sij", left_done, right_inv, precision=high)
    stacked = jnp.concatenate([grads_part, pre_part], axis=2)
    stacked = stacked.reshape(seq_count, tensor_size, row_width, 2 * proj_rank)
    stacked = stacked.transpose(1, 0, 2, 3)
    rows = jnp.sum(lax.all_to_all(stacked, "tensor", 0, 0, tiled=True), axis=0)
    grad_flat = rows[:, :, :proj_rank].reshape(seq_count, row_width * proj_rank)
    pre_flat = rows[:, :, proj_rank:].reshape(seq_count, row_width * proj_rank)
    lang_total = owner.shape[0]
    dp_size = lax.axis_size("dp")
    slot_count = (lang_total + dp_size - 1) // dp_size
    owned_rows = slot_count * dp_size
    lang_index = jnp.arange(lang_total, dtype=jnp.int32)
    same_owner = (owner[:, None] == owner[None, :]) & (lang_index[None, :] < lang_index[:, None])
    lang_slot = jnp.sum(same_owner.astype(jnp.int32), axis=1)
    lang_place = owner * slot_count + lang_slot
    lang_hot = (language[:, None] == lang_index[None, :]).astype(jnp.int32)
    seq_place = jnp.sum(lang_hot * lang_place[None, :], axis=1)
    slot_index = jnp.arange(owned_rows, dtype=jnp.int32).reshape(dp_size, slot_count)
    place_match = seq_place[:, None, None] == slot_index[None]
    slot_sums = jnp.sum(jnp.where(place_match[..., None], pre_flat[:, None, None, :], 0.0), axis=0)
    slot_counts = jnp.sum(place_match.astype(jnp.float32), axis=0)
    count_pad = 128
    payload = jnp.concatenate(
        [slot_sums, jnp.pad(slot_counts[:, :, None], ((0, 0), (0, 0), (0, count_pad - 1)))],
        axis=2,
    )
    gathered = jnp.sum(lax.all_to_all(payload, "dp", 0, 0, tiled=True), axis=0)
    width = pre_flat.shape[1]
    owned_means = gathered[:, :width] / jnp.maximum(gathered[:, width], 1.0)[:, None]
    return (grad_flat, owned_means)


def solution(mesh):
    return jax.shard_map(
        per_device,
        mesh=mesh,
        in_specs=(
            P("dp", None, "tensor"),
            P("dp", None, "tensor"),
            P(None, "tensor"),
            P(None, "tensor"),
            P(),
            P(),
            P("dp"),
            P("dp"),
            P(),
        ),
        out_specs=(P("dp", "tensor"), P("dp", "tensor")),
        check_vma=False,
    )
```

```python
import jax
import jax.numpy as jnp
from jax import lax
from jax.experimental import pallas as pl
from jax.sharding import PartitionSpec as P


def _project_kernel(hidden_ref, grad_ref, proj_in_ref, proj_out_ref, out_ref):
    contract = (((1,), (1,)), ((), ()))
    rank = proj_in_ref.shape[0]
    out_ref[:, :rank] = lax.dot_general(
        hidden_ref[...], proj_in_ref[...], contract, preferred_element_type=jnp.float32
    )
    out_ref[:, rank:] = lax.dot_general(
        grad_ref[...], proj_out_ref[...], contract, preferred_element_type=jnp.float32
    )


def project_both(hidden, out_grad, proj_in, proj_out, tile):
    hidden = hidden.reshape(-1, hidden.shape[-1])
    out_grad = out_grad.reshape(-1, out_grad.shape[-1])
    tokens = hidden.shape[0]
    rank = proj_in.shape[0]
    return pl.pallas_call(
        _project_kernel,
        grid=(tokens // tile,),
        in_specs=[
            pl.BlockSpec((tile, hidden.shape[1]), lambda i: (i, 0)),
            pl.BlockSpec((tile, out_grad.shape[1]), lambda i: (i, 0)),
            pl.BlockSpec(proj_in.shape, lambda i: (0, 0)),
            pl.BlockSpec(proj_out.shape, lambda i: (0, 0)),
        ],
        out_specs=pl.BlockSpec((tile, 2 * rank), lambda i: (i, 0)),
        out_shape=jax.ShapeDtypeStruct((tokens, 2 * rank), jnp.float32),
    )(hidden, out_grad, proj_in, proj_out)


def _block_kernel(recv_ref, weight_ref, left_inv_ref, right_inv_ref, out_ref):
    peers, _, double = recv_ref.shape
    rank = double // 2
    _, seqs, width, _ = out_ref.shape
    total = recv_ref[0]
    for peer in range(1, peers):
        total = total + recv_ref[peer]
    left = total[:, :rank]
    right = total[:, rank:]
    highest = lax.Precision.HIGHEST
    for s in range(seqs):
        right_s = right * weight_ref[:, s : s + 1]
        grads = lax.dot_general(
            left, right_s, (((0,), (0,)), ((), ())), precision=highest,
            preferred_element_type=jnp.float32,
        )
        left_done = jnp.dot(left_inv_ref[...], grads, precision=highest,
                            preferred_element_type=jnp.float32)
        pre = jnp.dot(left_done, right_inv_ref[...], precision=highest,
                      preferred_element_type=jnp.float32)
        for k in range(peers):
            out_ref[k, s, :, :rank] = grads[k * width : (k + 1) * width, :]
            out_ref[k, s, :, rank:] = pre[k * width : (k + 1) * width, :]


def block_shares(recv, weight_t, left_inv, right_inv, seqs, width):
    peers, tokens, double = recv.shape
    return pl.pallas_call(
        _block_kernel,
        out_shape=jax.ShapeDtypeStruct((peers, seqs, width, double), jnp.float32),
    )(recv, weight_t, left_inv, right_inv)


def per_device(hidden, out_grad, proj_in, proj_out, left_inv, right_inv, lengths, language, owner):
    seq_count = hidden.shape[0]
    seq_length = hidden.shape[1]
    proj_rank = proj_in.shape[0]
    tensor_size = lax.axis_size("tensor")
    row_width = proj_rank // tensor_size
    parts = project_both(hidden, out_grad, proj_in, proj_out, seq_length)
    tokens = seq_count * seq_length
    block = tokens // tensor_size
    chunks = parts.reshape(tensor_size, block, 2 * proj_rank)
    recv = lax.all_to_all(chunks, "tensor", 0, 0, tiled=True)
    token_at = lax.axis_index("tensor") * block + jnp.arange(block, dtype=jnp.int32)
    token_seq = token_at // seq_length
    token_pos = token_at % seq_length
    seq_index = jnp.arange(seq_count, dtype=jnp.int32)
    weight = (token_seq[:, None] == seq_index[None, :]) & (token_pos[:, None] < lengths[None, :])
    stacked = block_shares(
        recv, weight.astype(jnp.float32), left_inv, right_inv, seq_count, row_width
    )
    rows = jnp.sum(lax.all_to_all(stacked, "tensor", 0, 0, tiled=True), axis=0)
    grad_flat = rows[:, :, :proj_rank].reshape(seq_count, row_width * proj_rank)
    pre_flat = rows[:, :, proj_rank:].reshape(seq_count, row_width * proj_rank)
    lang_total = owner.shape[0]
    dp_size = lax.axis_size("dp")
    slot_count = (lang_total + dp_size - 1) // dp_size
    owned_rows = slot_count * dp_size
    lang_index = jnp.arange(lang_total, dtype=jnp.int32)
    same_owner = (owner[:, None] == owner[None, :]) & (lang_index[None, :] < lang_index[:, None])
    lang_slot = jnp.sum(same_owner.astype(jnp.int32), axis=1)
    lang_place = owner * slot_count + lang_slot
    lang_hot = (language[:, None] == lang_index[None, :]).astype(jnp.int32)
    seq_place = jnp.sum(lang_hot * lang_place[None, :], axis=1)
    slot_index = jnp.arange(owned_rows, dtype=jnp.int32).reshape(dp_size, slot_count)
    place_match = seq_place[:, None, None] == slot_index[None]
    slot_sums = jnp.sum(jnp.where(place_match[..., None], pre_flat[:, None, None, :], 0.0), axis=0)
    slot_counts = jnp.sum(place_match.astype(jnp.float32), axis=0)
    count_pad = 128
    payload = jnp.concatenate(
        [slot_sums, jnp.pad(slot_counts[:, :, None], ((0, 0), (0, 0), (0, count_pad - 1)))],
        axis=2,
    )
    gathered = jnp.sum(lax.all_to_all(payload, "dp", 0, 0, tiled=True), axis=0)
    width = pre_flat.shape[1]
    owned_means = gathered[:, :width] / jnp.maximum(gathered[:, width], 1.0)[:, None]
    return (grad_flat, owned_means)


def solution(mesh):
    return jax.shard_map(
        per_device,
        mesh=mesh,
        in_specs=(
            P("dp", None, "tensor"),
            P("dp", None, "tensor"),
            P(None, "tensor"),
            P(None, "tensor"),
            P(),
            P(),
            P("dp"),
            P("dp"),
            P(),
        ),
        out_specs=(P("dp", "tensor"), P("dp", "tensor")),
        check_vma=False,
    )
```

```python
import jax
import jax.numpy as jnp
from jax import lax
from jax.experimental import pallas as pl
from jax.sharding import PartitionSpec as P


def _project_kernel(hidden_ref, grad_ref, proj_in_ref, proj_out_ref, out_ref):
    contract = (((1,), (1,)), ((), ()))
    rank = proj_in_ref.shape[0]
    out_ref[:, :rank] = lax.dot_general(
        hidden_ref[...], proj_in_ref[...], contract, preferred_element_type=jnp.float32
    )
    out_ref[:, rank:] = lax.dot_general(
        grad_ref[...], proj_out_ref[...], contract, preferred_element_type=jnp.float32
    )


def project_both(hidden, out_grad, proj_in, proj_out, tile):
    hidden = hidden.reshape(-1, hidden.shape[-1])
    out_grad = out_grad.reshape(-1, out_grad.shape[-1])
    tokens = hidden.shape[0]
    rank = proj_in.shape[0]
    return pl.pallas_call(
        _project_kernel,
        grid=(tokens // tile,),
        in_specs=[
            pl.BlockSpec((tile, hidden.shape[1]), lambda i: (i, 0)),
            pl.BlockSpec((tile, out_grad.shape[1]), lambda i: (i, 0)),
            pl.BlockSpec(proj_in.shape, lambda i: (0, 0)),
            pl.BlockSpec(proj_out.shape, lambda i: (0, 0)),
        ],
        out_specs=pl.BlockSpec((tile, 2 * rank), lambda i: (i, 0)),
        out_shape=jax.ShapeDtypeStruct((tokens, 2 * rank), jnp.float32),
    )(hidden, out_grad, proj_in, proj_out)


def per_device(hidden, out_grad, proj_in, proj_out, left_inv, right_inv, lengths, language, owner):
    high = lax.Precision.HIGH
    seq_count = hidden.shape[0]
    seq_length = hidden.shape[1]
    proj_rank = proj_in.shape[0]
    tensor_size = lax.axis_size("tensor")
    row_width = proj_rank // tensor_size
    parts = project_both(hidden, out_grad, proj_in, proj_out, seq_count * seq_length)
    tokens = seq_count * seq_length
    block = tokens // tensor_size
    chunks = parts.reshape(tensor_size, block, 2 * proj_rank)
    mine = jnp.sum(lax.all_to_all(chunks, "tensor", 0, 0, tiled=True), axis=0)
    token_at = lax.axis_index("tensor") * block + jnp.arange(block, dtype=jnp.int32)
    token_seq = token_at // seq_length
    token_pos = token_at % seq_length
    seq_index = jnp.arange(seq_count, dtype=jnp.int32)
    weight = (token_seq[None, :] == seq_index[:, None]) & (token_pos[None, :] < lengths[:, None])
    right_seq = mine[None, :, proj_rank:] * weight.astype(jnp.float32)[:, :, None]
    grads_part = jnp.einsum("ti,stj->sij", mine[:, :proj_rank], right_seq, precision=high)
    left_done = jnp.einsum("ik,skj->sij", left_inv, grads_part, precision=high)
    pre_part = jnp.einsum("sik,kj->sij", left_done, right_inv, precision=high)
    stacked = jnp.concatenate([grads_part, pre_part], axis=2)
    stacked = stacked.reshape(seq_count, tensor_size, row_width, 2 * proj_rank)
    stacked = stacked.transpose(1, 0, 2, 3)
    rows = jnp.sum(lax.all_to_all(stacked, "tensor", 0, 0, tiled=True), axis=0)
    grad_flat = rows[:, :, :proj_rank].reshape(seq_count, row_width * proj_rank)
    pre_flat = rows[:, :, proj_rank:].reshape(seq_count, row_width * proj_rank)
    lang_total = owner.shape[0]
    dp_size = lax.axis_size("dp")
    slot_count = (lang_total + dp_size - 1) // dp_size
    owned_rows = slot_count * dp_size
    lang_index = jnp.arange(lang_total, dtype=jnp.int32)
    same_owner = (owner[:, None] == owner[None, :]) & (lang_index[None, :] < lang_index[:, None])
    lang_slot = jnp.sum(same_owner.astype(jnp.int32), axis=1)
    lang_place = owner * slot_count + lang_slot
    lang_hot = (language[:, None] == lang_index[None, :]).astype(jnp.int32)
    seq_place = jnp.sum(lang_hot * lang_place[None, :], axis=1)
    slot_index = jnp.arange(owned_rows, dtype=jnp.int32).reshape(dp_size, slot_count)
    place_match = seq_place[:, None, None] == slot_index[None]
    slot_sums = jnp.sum(jnp.where(place_match[..., None], pre_flat[:, None, None, :], 0.0), axis=0)
    slot_counts = jnp.sum(place_match.astype(jnp.float32), axis=0)
    count_pad = 128
    payload = jnp.concatenate(
        [slot_sums, jnp.pad(slot_counts[:, :, None], ((0, 0), (0, 0), (0, count_pad - 1)))],
        axis=2,
    )
    gathered = jnp.sum(lax.all_to_all(payload, "dp", 0, 0, tiled=True), axis=0)
    width = pre_flat.shape[1]
    owned_means = gathered[:, :width] / jnp.maximum(gathered[:, width], 1.0)[:, None]
    return (grad_flat, owned_means)


def solution(mesh):
    return jax.shard_map(
        per_device,
        mesh=mesh,
        in_specs=(
            P("dp", None, "tensor"),
            P("dp", None, "tensor"),
            P(None, "tensor"),
            P(None, "tensor"),
            P(),
            P(),
            P("dp"),
            P("dp"),
            P(),
        ),
        out_specs=(P("dp", "tensor"), P("dp", "tensor")),
        check_vma=False,
    )
```

```python
import jax
import jax.numpy as jnp
from jax import lax
from jax.experimental import pallas as pl
from jax.sharding import PartitionSpec as P


def _project_kernel(hidden_ref, grad_ref, proj_in_ref, proj_out_ref, out_ref):
    contract = (((1,), (1,)), ((), ()))
    rank = proj_in_ref.shape[0]
    out_ref[:, :rank] = lax.dot_general(
        hidden_ref[...], proj_in_ref[...], contract, preferred_element_type=jnp.float32
    )
    out_ref[:, rank:] = lax.dot_general(
        grad_ref[...], proj_out_ref[...], contract, preferred_element_type=jnp.float32
    )


def project_both(hidden, out_grad, proj_in, proj_out, tile):
    hidden = hidden.reshape(-1, hidden.shape[-1])
    out_grad = out_grad.reshape(-1, out_grad.shape[-1])
    tokens = hidden.shape[0]
    rank = proj_in.shape[0]
    return pl.pallas_call(
        _project_kernel,
        grid=(tokens // tile,),
        in_specs=[
            pl.BlockSpec((tile, hidden.shape[1]), lambda i: (i, 0)),
            pl.BlockSpec((tile, out_grad.shape[1]), lambda i: (i, 0)),
            pl.BlockSpec(proj_in.shape, lambda i: (0, 0)),
            pl.BlockSpec(proj_out.shape, lambda i: (0, 0)),
        ],
        out_specs=pl.BlockSpec((tile, 2 * rank), lambda i: (i, 0)),
        out_shape=jax.ShapeDtypeStruct((tokens, 2 * rank), jnp.float32),
    )(hidden, out_grad, proj_in, proj_out)


def per_device(hidden, out_grad, proj_in, proj_out, left_inv, right_inv, lengths, language, owner):
    high = lax.Precision.HIGH
    seq_count = hidden.shape[0]
    seq_length = hidden.shape[1]
    proj_rank = proj_in.shape[0]
    tensor_size = lax.axis_size("tensor")
    row_width = proj_rank // tensor_size
    parts = project_both(hidden, out_grad, proj_in, proj_out, seq_count * seq_length // 2)
    tokens = seq_count * seq_length
    block = tokens // tensor_size
    chunks = parts.reshape(tensor_size, block, 2 * proj_rank)
    mine = jnp.sum(lax.all_to_all(chunks, "tensor", 0, 0, tiled=True), axis=0)
    token_at = lax.axis_index("tensor") * block + jnp.arange(block, dtype=jnp.int32)
    token_seq = token_at // seq_length
    token_pos = token_at % seq_length
    seq_index = jnp.arange(seq_count, dtype=jnp.int32)
    weight = (token_seq[None, :] == seq_index[:, None]) & (token_pos[None, :] < lengths[:, None])
    right_seq = mine[None, :, proj_rank:] * weight.astype(jnp.float32)[:, :, None]
    grads_part = jnp.einsum("ti,stj->sij", mine[:, :proj_rank], right_seq, precision=high)
    left_done = jnp.einsum("ik,skj->sij", left_inv, grads_part, precision=high)
    pre_part = jnp.einsum("sik,kj->sij", left_done, right_inv, precision=high)
    stacked = jnp.concatenate([grads_part, pre_part], axis=2)
    stacked = stacked.reshape(seq_count, tensor_size, row_width, 2 * proj_rank)
    stacked = stacked.transpose(1, 0, 2, 3)
    rows = jnp.sum(lax.all_to_all(stacked, "tensor", 0, 0, tiled=True), axis=0)
    grad_flat = rows[:, :, :proj_rank].reshape(seq_count, row_width * proj_rank)
    pre_flat = rows[:, :, proj_rank:].reshape(seq_count, row_width * proj_rank)
    lang_total = owner.shape[0]
    dp_size = lax.axis_size("dp")
    slot_count = (lang_total + dp_size - 1) // dp_size
    owned_rows = slot_count * dp_size
    lang_index = jnp.arange(lang_total, dtype=jnp.int32)
    same_owner = (owner[:, None] == owner[None, :]) & (lang_index[None, :] < lang_index[:, None])
    lang_slot = jnp.sum(same_owner.astype(jnp.int32), axis=1)
    lang_place = owner * slot_count + lang_slot
    lang_hot = (language[:, None] == lang_index[None, :]).astype(jnp.int32)
    seq_place = jnp.sum(lang_hot * lang_place[None, :], axis=1)
    slot_index = jnp.arange(owned_rows, dtype=jnp.int32).reshape(dp_size, slot_count)
    place_match = seq_place[:, None, None] == slot_index[None]
    slot_sums = jnp.sum(jnp.where(place_match[..., None], pre_flat[:, None, None, :], 0.0), axis=0)
    slot_counts = jnp.sum(place_match.astype(jnp.float32), axis=0)
    count_pad = 128
    payload = jnp.concatenate(
        [slot_sums, jnp.pad(slot_counts[:, :, None], ((0, 0), (0, 0), (0, count_pad - 1)))],
        axis=2,
    )
    gathered = jnp.sum(lax.all_to_all(payload, "dp", 0, 0, tiled=True), axis=0)
    width = pre_flat.shape[1]
    owned_means = gathered[:, :width] / jnp.maximum(gathered[:, width], 1.0)[:, None]
    return (grad_flat, owned_means)


def solution(mesh):
    return jax.shard_map(
        per_device,
        mesh=mesh,
        in_specs=(
            P("dp", None, "tensor"),
            P("dp", None, "tensor"),
            P(None, "tensor"),
            P(None, "tensor"),
            P(),
            P(),
            P("dp"),
            P("dp"),
            P(),
        ),
        out_specs=(P("dp", "tensor"), P("dp", "tensor")),
        check_vma=False,
    )
```

```python
import jax
import jax.numpy as jnp
from jax import lax
from jax.experimental import pallas as pl
from jax.sharding import PartitionSpec as P


def _project_kernel(hidden_ref, grad_ref, proj_in_ref, proj_out_ref, out_ref):
    contract = (((1,), (1,)), ((), ()))
    rank = proj_in_ref.shape[0]
    out_ref[:, :rank] = lax.dot_general(
        hidden_ref[...], proj_in_ref[...], contract, preferred_element_type=jnp.float32
    )
    out_ref[:, rank:] = lax.dot_general(
        grad_ref[...], proj_out_ref[...], contract, preferred_element_type=jnp.float32
    )


def project_both(hidden, out_grad, proj_in, proj_out, tile):
    hidden = hidden.reshape(-1, hidden.shape[-1])
    out_grad = out_grad.reshape(-1, out_grad.shape[-1])
    tokens = hidden.shape[0]
    rank = proj_in.shape[0]
    return pl.pallas_call(
        _project_kernel,
        grid=(tokens // tile,),
        in_specs=[
            pl.BlockSpec((tile, hidden.shape[1]), lambda i: (i, 0)),
            pl.BlockSpec((tile, out_grad.shape[1]), lambda i: (i, 0)),
            pl.BlockSpec(proj_in.shape, lambda i: (0, 0)),
            pl.BlockSpec(proj_out.shape, lambda i: (0, 0)),
        ],
        out_specs=pl.BlockSpec((tile, 2 * rank), lambda i: (i, 0)),
        out_shape=jax.ShapeDtypeStruct((tokens, 2 * rank), jnp.float32),
    )(hidden, out_grad, proj_in, proj_out)


def per_device(hidden, out_grad, proj_in, proj_out, left_inv, right_inv, lengths, language, owner):
    high = lax.Precision.HIGH
    seq_count = hidden.shape[0]
    seq_length = hidden.shape[1]
    proj_rank = proj_in.shape[0]
    tensor_size = lax.axis_size("tensor")
    row_width = proj_rank // tensor_size
    parts = project_both(hidden, out_grad, proj_in, proj_out, seq_count * seq_length // 4)
    tokens = seq_count * seq_length
    block = tokens // tensor_size
    chunks = parts.reshape(tensor_size, block, 2 * proj_rank)
    mine = jnp.sum(lax.all_to_all(chunks, "tensor", 0, 0, tiled=True), axis=0)
    token_at = lax.axis_index("tensor") * block + jnp.arange(block, dtype=jnp.int32)
    token_seq = token_at // seq_length
    token_pos = token_at % seq_length
    seq_index = jnp.arange(seq_count, dtype=jnp.int32)
    weight = (token_seq[None, :] == seq_index[:, None]) & (token_pos[None, :] < lengths[:, None])
    right_seq = mine[None, :, proj_rank:] * weight.astype(jnp.float32)[:, :, None]
    grads_part = jnp.einsum("ti,stj->sij", mine[:, :proj_rank], right_seq, precision=high)
    left_done = jnp.einsum("ik,skj->sij", left_inv, grads_part, precision=high)
    pre_part = jnp.einsum("sik,kj->sij", left_done, right_inv, precision=high)
    stacked = jnp.concatenate([grads_part, pre_part], axis=2)
    stacked = stacked.reshape(seq_count, tensor_size, row_width, 2 * proj_rank)
    stacked = stacked.transpose(1, 0, 2, 3)
    rows = jnp.sum(lax.all_to_all(stacked, "tensor", 0, 0, tiled=True), axis=0)
    grad_flat = rows[:, :, :proj_rank].reshape(seq_count, row_width * proj_rank)
    pre_flat = rows[:, :, proj_rank:].reshape(seq_count, row_width * proj_rank)
    lang_total = owner.shape[0]
    dp_size = lax.axis_size("dp")
    slot_count = (lang_total + dp_size - 1) // dp_size
    owned_rows = slot_count * dp_size
    lang_index = jnp.arange(lang_total, dtype=jnp.int32)
    same_owner = (owner[:, None] == owner[None, :]) & (lang_index[None, :] < lang_index[:, None])
    lang_slot = jnp.sum(same_owner.astype(jnp.int32), axis=1)
    lang_place = owner * slot_count + lang_slot
    lang_hot = (language[:, None] == lang_index[None, :]).astype(jnp.int32)
    seq_place = jnp.sum(lang_hot * lang_place[None, :], axis=1)
    slot_index = jnp.arange(owned_rows, dtype=jnp.int32).reshape(dp_size, slot_count)
    place_match = seq_place[:, None, None] == slot_index[None]
    slot_sums = jnp.sum(jnp.where(place_match[..., None], pre_flat[:, None, None, :], 0.0), axis=0)
    slot_counts = jnp.sum(place_match.astype(jnp.float32), axis=0)
    count_pad = 128
    payload = jnp.concatenate(
        [slot_sums, jnp.pad(slot_counts[:, :, None], ((0, 0), (0, 0), (0, count_pad - 1)))],
        axis=2,
    )
    gathered = jnp.sum(lax.all_to_all(payload, "dp", 0, 0, tiled=True), axis=0)
    width = pre_flat.shape[1]
    owned_means = gathered[:, :width] / jnp.maximum(gathered[:, width], 1.0)[:, None]
    return (grad_flat, owned_means)


def solution(mesh):
    return jax.shard_map(
        per_device,
        mesh=mesh,
        in_specs=(
            P("dp", None, "tensor"),
            P("dp", None, "tensor"),
            P(None, "tensor"),
            P(None, "tensor"),
            P(),
            P(),
            P("dp"),
            P("dp"),
            P(),
        ),
        out_specs=(P("dp", "tensor"), P("dp", "tensor")),
        check_vma=False,
    )
```

```python
import jax
import jax.numpy as jnp
from jax import lax
from jax.experimental import pallas as pl
from jax.sharding import PartitionSpec as P


def _project_kernel(hidden_ref, grad_ref, proj_in_ref, proj_out_ref, out_ref):
    contract = (((1,), (1,)), ((), ()))
    rank = proj_in_ref.shape[0]
    out_ref[:, :rank] = lax.dot_general(
        hidden_ref[...], proj_in_ref[...], contract, preferred_element_type=jnp.float32
    )
    out_ref[:, rank:] = lax.dot_general(
        grad_ref[...], proj_out_ref[...], contract, preferred_element_type=jnp.float32
    )


def project_both(hidden, out_grad, proj_in, proj_out, tile):
    hidden = hidden.reshape(-1, hidden.shape[-1])
    out_grad = out_grad.reshape(-1, out_grad.shape[-1])
    tokens = hidden.shape[0]
    rank = proj_in.shape[0]
    return pl.pallas_call(
        _project_kernel,
        grid=(tokens // tile,),
        in_specs=[
            pl.BlockSpec((tile, hidden.shape[1]), lambda i: (i, 0)),
            pl.BlockSpec((tile, out_grad.shape[1]), lambda i: (i, 0)),
            pl.BlockSpec(proj_in.shape, lambda i: (0, 0)),
            pl.BlockSpec(proj_out.shape, lambda i: (0, 0)),
        ],
        out_specs=pl.BlockSpec((tile, 2 * rank), lambda i: (i, 0)),
        out_shape=jax.ShapeDtypeStruct((tokens, 2 * rank), jnp.float32),
    )(hidden, out_grad, proj_in, proj_out)


def per_device(hidden, out_grad, proj_in, proj_out, left_inv, right_inv, lengths, language, owner):
    high = lax.Precision.HIGH
    seq_count = hidden.shape[0]
    seq_length = hidden.shape[1]
    proj_rank = proj_in.shape[0]
    tensor_size = lax.axis_size("tensor")
    row_width = proj_rank // tensor_size
    parts = project_both(hidden, out_grad, proj_in, proj_out, seq_count * seq_length // 2)
    tokens = seq_count * seq_length
    block = tokens // tensor_size
    chunks = parts.reshape(tensor_size, block, 2 * proj_rank)
    mine = jnp.sum(lax.all_to_all(chunks, "tensor", 0, 0, tiled=True), axis=0)
    token_at = lax.axis_index("tensor") * block + jnp.arange(block, dtype=jnp.int32)
    token_seq = token_at // seq_length
    token_pos = token_at % seq_length
    seq_index = jnp.arange(seq_count, dtype=jnp.int32)
    weight = (token_seq[None, :] == seq_index[:, None]) & (token_pos[None, :] < lengths[:, None])
    upper = (jnp.arange(2 * proj_rank, dtype=jnp.int32) >= proj_rank).astype(jnp.float32)
    right_seq = mine[None, :, :] * (weight.astype(jnp.float32)[:, :, None] * upper[None, None, :])
    grads_part = jnp.einsum("ti,stj->sij", mine[:, :proj_rank], right_seq, precision=high)
    left_done = jnp.einsum("ik,skj->sij", left_inv, grads_part, precision=high)
    to_lower = jnp.zeros((2 * proj_rank, 2 * proj_rank), jnp.float32)
    to_lower = to_lower.at[proj_rank:, :proj_rank].set(right_inv)
    pre_part = jnp.einsum("sik,kj->sij", left_done, to_lower, precision=high)
    stacked = (grads_part + pre_part).reshape(seq_count, tensor_size, row_width, 2 * proj_rank)
    stacked = stacked.transpose(1, 0, 2, 3)
    rows = jnp.sum(lax.all_to_all(stacked, "tensor", 0, 0, tiled=True), axis=0)
    grad_flat = rows[:, :, proj_rank:].reshape(seq_count, row_width * proj_rank)
    pre_flat = rows[:, :, :proj_rank].reshape(seq_count, row_width * proj_rank)
    lang_total = owner.shape[0]
    dp_size = lax.axis_size("dp")
    slot_count = (lang_total + dp_size - 1) // dp_size
    owned_rows = slot_count * dp_size
    lang_index = jnp.arange(lang_total, dtype=jnp.int32)
    same_owner = (owner[:, None] == owner[None, :]) & (lang_index[None, :] < lang_index[:, None])
    lang_slot = jnp.sum(same_owner.astype(jnp.int32), axis=1)
    lang_place = owner * slot_count + lang_slot
    lang_hot = (language[:, None] == lang_index[None, :]).astype(jnp.int32)
    seq_place = jnp.sum(lang_hot * lang_place[None, :], axis=1)
    slot_index = jnp.arange(owned_rows, dtype=jnp.int32).reshape(dp_size, slot_count)
    place_match = seq_place[:, None, None] == slot_index[None]
    slot_sums = jnp.sum(jnp.where(place_match[..., None], pre_flat[:, None, None, :], 0.0), axis=0)
    slot_counts = jnp.sum(place_match.astype(jnp.float32), axis=0)
    count_pad = 128
    payload = jnp.concatenate(
        [slot_sums, jnp.pad(slot_counts[:, :, None], ((0, 0), (0, 0), (0, count_pad - 1)))],
        axis=2,
    )
    gathered = jnp.sum(lax.all_to_all(payload, "dp", 0, 0, tiled=True), axis=0)
    width = pre_flat.shape[1]
    owned_means = gathered[:, :width] / jnp.maximum(gathered[:, width], 1.0)[:, None]
    return (grad_flat, owned_means)


def solution(mesh):
    return jax.shard_map(
        per_device,
        mesh=mesh,
        in_specs=(
            P("dp", None, "tensor"),
            P("dp", None, "tensor"),
            P(None, "tensor"),
            P(None, "tensor"),
            P(),
            P(),
            P("dp"),
            P("dp"),
            P(),
        ),
        out_specs=(P("dp", "tensor"), P("dp", "tensor")),
        check_vma=False,
    )
```

```python
import jax
import jax.numpy as jnp
from jax import lax
from jax.experimental import pallas as pl
from jax.sharding import PartitionSpec as P


def _project_kernel(hidden_ref, grad_ref, proj_in_ref, proj_out_ref, out_ref):
    contract = (((1,), (1,)), ((), ()))
    rank = proj_in_ref.shape[0]
    out_ref[:, :rank] = lax.dot_general(
        hidden_ref[...], proj_in_ref[...], contract, preferred_element_type=jnp.float32
    )
    out_ref[:, rank:] = lax.dot_general(
        grad_ref[...], proj_out_ref[...], contract, preferred_element_type=jnp.float32
    )


def project_both(hidden, out_grad, proj_in, proj_out, tile):
    hidden = hidden.reshape(-1, hidden.shape[-1])
    out_grad = out_grad.reshape(-1, out_grad.shape[-1])
    tokens = hidden.shape[0]
    rank = proj_in.shape[0]
    return pl.pallas_call(
        _project_kernel,
        grid=(tokens // tile,),
        in_specs=[
            pl.BlockSpec((tile, hidden.shape[1]), lambda i: (i, 0)),
            pl.BlockSpec((tile, out_grad.shape[1]), lambda i: (i, 0)),
            pl.BlockSpec(proj_in.shape, lambda i: (0, 0)),
            pl.BlockSpec(proj_out.shape, lambda i: (0, 0)),
        ],
        out_specs=pl.BlockSpec((tile, 2 * rank), lambda i: (i, 0)),
        out_shape=jax.ShapeDtypeStruct((tokens, 2 * rank), jnp.float32),
    )(hidden, out_grad, proj_in, proj_out)


def per_device(hidden, out_grad, proj_in, proj_out, left_inv, right_inv, lengths, language, owner):
    high = lax.Precision.HIGH
    seq_count = hidden.shape[0]
    seq_length = hidden.shape[1]
    proj_rank = proj_in.shape[0]
    tensor_size = lax.axis_size("tensor")
    row_width = proj_rank // tensor_size
    parts = project_both(hidden, out_grad, proj_in, proj_out, seq_count * seq_length // 2)
    tokens = seq_count * seq_length
    block = tokens // tensor_size
    chunks = parts.reshape(tensor_size, block, 2 * proj_rank)
    mine = jnp.sum(lax.all_to_all(chunks, "tensor", 0, 0, tiled=True), axis=0)
    token_at = lax.axis_index("tensor") * block + jnp.arange(block, dtype=jnp.int32)
    token_seq = token_at // seq_length
    token_pos = token_at % seq_length
    seq_index = jnp.arange(seq_count, dtype=jnp.int32)
    weight = (token_seq[None, :] == seq_index[:, None]) & (token_pos[None, :] < lengths[:, None])
    double = 2 * proj_rank
    upper = (jnp.arange(double, dtype=jnp.int32) >= proj_rank).astype(jnp.float32)
    right_seq = mine[:, None, :] * (weight.T.astype(jnp.float32)[:, :, None] * upper[None, None, :])
    right_seq = right_seq.reshape(block, seq_count * double)
    grads_part = lax.dot_general(
        mine[:, :proj_rank], right_seq, (((0,), (0,)), ((), ())), precision=high
    )
    left_done = jnp.dot(left_inv, grads_part, precision=high)
    to_lower = jnp.zeros((double, double), jnp.float32)
    to_lower = to_lower.at[proj_rank:, :proj_rank].set(right_inv)
    to_lower = jnp.kron(jnp.eye(seq_count, dtype=jnp.float32), to_lower)
    pre_part = jnp.dot(left_done, to_lower, precision=high)
    stacked = (grads_part + pre_part).reshape(tensor_size, row_width, seq_count * double)
    rows = jnp.sum(lax.all_to_all(stacked, "tensor", 0, 0, tiled=True), axis=0)
    rows = rows.reshape(row_width, seq_count, double).transpose(1, 0, 2)
    grad_flat = rows[:, :, proj_rank:].reshape(seq_count, row_width * proj_rank)
    pre_flat = rows[:, :, :proj_rank].reshape(seq_count, row_width * proj_rank)
    lang_total = owner.shape[0]
    dp_size = lax.axis_size("dp")
    slot_count = (lang_total + dp_size - 1) // dp_size
    owned_rows = slot_count * dp_size
    lang_index = jnp.arange(lang_total, dtype=jnp.int32)
    same_owner = (owner[:, None] == owner[None, :]) & (lang_index[None, :] < lang_index[:, None])
    lang_slot = jnp.sum(same_owner.astype(jnp.int32), axis=1)
    lang_place = owner * slot_count + lang_slot
    lang_hot = (language[:, None] == lang_index[None, :]).astype(jnp.int32)
    seq_place = jnp.sum(lang_hot * lang_place[None, :], axis=1)
    slot_index = jnp.arange(owned_rows, dtype=jnp.int32).reshape(dp_size, slot_count)
    place_match = seq_place[:, None, None] == slot_index[None]
    slot_sums = jnp.sum(jnp.where(place_match[..., None], pre_flat[:, None, None, :], 0.0), axis=0)
    slot_counts = jnp.sum(place_match.astype(jnp.float32), axis=0)
    count_pad = 128
    payload = jnp.concatenate(
        [slot_sums, jnp.pad(slot_counts[:, :, None], ((0, 0), (0, 0), (0, count_pad - 1)))],
        axis=2,
    )
    gathered = jnp.sum(lax.all_to_all(payload, "dp", 0, 0, tiled=True), axis=0)
    width = pre_flat.shape[1]
    owned_means = gathered[:, :width] / jnp.maximum(gathered[:, width], 1.0)[:, None]
    return (grad_flat, owned_means)


def solution(mesh):
    return jax.shard_map(
        per_device,
        mesh=mesh,
        in_specs=(
            P("dp", None, "tensor"),
            P("dp", None, "tensor"),
            P(None, "tensor"),
            P(None, "tensor"),
            P(),
            P(),
            P("dp"),
            P("dp"),
            P(),
        ),
        out_specs=(P("dp", "tensor"), P("dp", "tensor")),
        check_vma=False,
    )
```

```python
import jax
import jax.numpy as jnp
from jax import lax
from jax.experimental import pallas as pl
from jax.sharding import PartitionSpec as P


def _project_kernel(hidden_ref, grad_ref, proj_in_ref, proj_out_ref, out_ref):
    contract = (((1,), (1,)), ((), ()))
    rank = proj_in_ref.shape[0]
    out_ref[:, :rank] = lax.dot_general(
        hidden_ref[...], proj_in_ref[...], contract, preferred_element_type=jnp.float32
    )
    out_ref[:, rank:] = lax.dot_general(
        grad_ref[...], proj_out_ref[...], contract, preferred_element_type=jnp.float32
    )


def project_both(hidden, out_grad, proj_in, proj_out, tile):
    hidden = hidden.reshape(-1, hidden.shape[-1])
    out_grad = out_grad.reshape(-1, out_grad.shape[-1])
    tokens = hidden.shape[0]
    rank = proj_in.shape[0]
    return pl.pallas_call(
        _project_kernel,
        grid=(tokens // tile,),
        in_specs=[
            pl.BlockSpec((tile, hidden.shape[1]), lambda i: (i, 0)),
            pl.BlockSpec((tile, out_grad.shape[1]), lambda i: (i, 0)),
            pl.BlockSpec(proj_in.shape, lambda i: (0, 0)),
            pl.BlockSpec(proj_out.shape, lambda i: (0, 0)),
        ],
        out_specs=pl.BlockSpec((tile, 2 * rank), lambda i: (i, 0)),
        out_shape=jax.ShapeDtypeStruct((tokens, 2 * rank), jnp.float32),
    )(hidden, out_grad, proj_in, proj_out)


def per_device(hidden, out_grad, proj_in, proj_out, left_inv, right_inv, lengths, language, owner):
    high = lax.Precision.HIGH
    seq_count = hidden.shape[0]
    seq_length = hidden.shape[1]
    proj_rank = proj_in.shape[0]
    tensor_size = lax.axis_size("tensor")
    row_width = proj_rank // tensor_size
    parts = project_both(hidden, out_grad, proj_in, proj_out, seq_count * seq_length // 2)
    tokens = seq_count * seq_length
    block = tokens // tensor_size
    chunks = parts.reshape(tensor_size, block, 2 * proj_rank)
    mine = jnp.sum(lax.all_to_all(chunks, "tensor", 0, 0, tiled=True), axis=0)
    token_at = lax.axis_index("tensor") * block + jnp.arange(block, dtype=jnp.int32)
    token_seq = token_at // seq_length
    token_pos = token_at % seq_length
    seq_index = jnp.arange(seq_count, dtype=jnp.int32)
    weight = (token_seq[None, :] == seq_index[:, None]) & (token_pos[None, :] < lengths[:, None])
    double = 2 * proj_rank
    right_blk = mine[:, proj_rank:]
    right_both = jnp.concatenate([jnp.dot(right_blk, right_inv, precision=high), right_blk], axis=1)
    right_seq = right_both[:, None, :] * weight.T.astype(jnp.float32)[:, :, None]
    right_seq = right_seq.reshape(block, seq_count * double)
    grads_part = lax.dot_general(
        mine[:, :proj_rank], right_seq, (((0,), (0,)), ((), ())), precision=high
    )
    left_done = jnp.dot(left_inv, grads_part, precision=high)
    lane = jnp.arange(seq_count * double, dtype=jnp.int32) % double
    shares = jnp.where(lane[None, :] < proj_rank, left_done, grads_part)
    stacked = shares.reshape(tensor_size, row_width, seq_count * double)
    rows = jnp.sum(lax.all_to_all(stacked, "tensor", 0, 0, tiled=True), axis=0)
    rows = rows.reshape(row_width, seq_count, double).transpose(1, 0, 2)
    grad_flat = rows[:, :, proj_rank:].reshape(seq_count, row_width * proj_rank)
    pre_flat = rows[:, :, :proj_rank].reshape(seq_count, row_width * proj_rank)
    lang_total = owner.shape[0]
    dp_size = lax.axis_size("dp")
    slot_count = (lang_total + dp_size - 1) // dp_size
    owned_rows = slot_count * dp_size
    lang_index = jnp.arange(lang_total, dtype=jnp.int32)
    same_owner = (owner[:, None] == owner[None, :]) & (lang_index[None, :] < lang_index[:, None])
    lang_slot = jnp.sum(same_owner.astype(jnp.int32), axis=1)
    lang_place = owner * slot_count + lang_slot
    lang_hot = (language[:, None] == lang_index[None, :]).astype(jnp.int32)
    seq_place = jnp.sum(lang_hot * lang_place[None, :], axis=1)
    slot_index = jnp.arange(owned_rows, dtype=jnp.int32).reshape(dp_size, slot_count)
    place_match = seq_place[:, None, None] == slot_index[None]
    slot_sums = jnp.sum(jnp.where(place_match[..., None], pre_flat[:, None, None, :], 0.0), axis=0)
    slot_counts = jnp.sum(place_match.astype(jnp.float32), axis=0)
    count_pad = 128
    payload = jnp.concatenate(
        [slot_sums, jnp.pad(slot_counts[:, :, None], ((0, 0), (0, 0), (0, count_pad - 1)))],
        axis=2,
    )
    gathered = jnp.sum(lax.all_to_all(payload, "dp", 0, 0, tiled=True), axis=0)
    width = pre_flat.shape[1]
    owned_means = gathered[:, :width] / jnp.maximum(gathered[:, width], 1.0)[:, None]
    return (grad_flat, owned_means)


def solution(mesh):
    return jax.shard_map(
        per_device,
        mesh=mesh,
        in_specs=(
            P("dp", None, "tensor"),
            P("dp", None, "tensor"),
            P(None, "tensor"),
            P(None, "tensor"),
            P(),
            P(),
            P("dp"),
            P("dp"),
            P(),
        ),
        out_specs=(P("dp", "tensor"), P("dp", "tensor")),
        check_vma=False,
    )
```

```python
import jax
import jax.numpy as jnp
from jax import lax
from jax.experimental import pallas as pl
from jax.sharding import PartitionSpec as P


def _project_kernel(hidden_ref, grad_ref, proj_in_ref, proj_out_ref, out_ref):
    contract = (((1,), (1,)), ((), ()))
    rank = proj_in_ref.shape[0]
    out_ref[:, :rank] = lax.dot_general(
        hidden_ref[...], proj_in_ref[...], contract, preferred_element_type=jnp.float32
    )
    out_ref[:, rank:] = lax.dot_general(
        grad_ref[...], proj_out_ref[...], contract, preferred_element_type=jnp.float32
    )


def project_both(hidden, out_grad, proj_in, proj_out, tile):
    hidden = hidden.reshape(-1, hidden.shape[-1])
    out_grad = out_grad.reshape(-1, out_grad.shape[-1])
    tokens = hidden.shape[0]
    rank = proj_in.shape[0]
    return pl.pallas_call(
        _project_kernel,
        grid=(tokens // tile,),
        in_specs=[
            pl.BlockSpec((tile, hidden.shape[1]), lambda i: (i, 0)),
            pl.BlockSpec((tile, out_grad.shape[1]), lambda i: (i, 0)),
            pl.BlockSpec(proj_in.shape, lambda i: (0, 0)),
            pl.BlockSpec(proj_out.shape, lambda i: (0, 0)),
        ],
        out_specs=pl.BlockSpec((tile, 2 * rank), lambda i: (i, 0)),
        out_shape=jax.ShapeDtypeStruct((tokens, 2 * rank), jnp.float32),
    )(hidden, out_grad, proj_in, proj_out)


def per_device(hidden, out_grad, proj_in, proj_out, left_inv, right_inv, lengths, language, owner):
    high = lax.Precision.HIGH
    seq_count = hidden.shape[0]
    seq_length = hidden.shape[1]
    proj_rank = proj_in.shape[0]
    tensor_size = lax.axis_size("tensor")
    row_width = proj_rank // tensor_size
    parts = project_both(hidden, out_grad, proj_in, proj_out, seq_count * seq_length // 2)
    tokens = seq_count * seq_length
    block = tokens // tensor_size
    chunks = parts.reshape(tensor_size, block, 2 * proj_rank)
    mine = jnp.sum(lax.all_to_all(chunks, "tensor", 0, 0, tiled=True), axis=0)
    token_at = lax.axis_index("tensor") * block + jnp.arange(block, dtype=jnp.int32)
    token_seq = token_at // seq_length
    token_pos = token_at % seq_length
    seq_index = jnp.arange(seq_count, dtype=jnp.int32)
    weight = (token_seq[None, :] == seq_index[:, None]) & (token_pos[None, :] < lengths[:, None])
    double = 2 * proj_rank
    upper = (jnp.arange(double, dtype=jnp.int32) >= proj_rank).astype(jnp.float32)
    right_seq = mine[:, None, :] * (weight.T.astype(jnp.float32)[:, :, None] * upper[None, None, :])
    right_seq = right_seq.reshape(block, seq_count * double)
    grads_part = lax.dot_general(
        mine[:, :proj_rank], right_seq, (((0,), (0,)), ((), ())), precision=high
    )
    left_done = jnp.dot(left_inv, grads_part, precision=high)
    to_lower = jnp.zeros((double, double), jnp.float32)
    to_lower = to_lower.at[proj_rank:, :proj_rank].set(right_inv)
    pre_part = jnp.concatenate(
        [
            jnp.dot(left_done[:, s * double : (s + 1) * double], to_lower, precision=high)
            for s in range(seq_count)
        ],
        axis=1,
    )
    stacked = (grads_part + pre_part).reshape(tensor_size, row_width, seq_count * double)
    rows = jnp.sum(lax.all_to_all(stacked, "tensor", 0, 0, tiled=True), axis=0)
    rows = rows.reshape(row_width, seq_count, double).transpose(1, 0, 2)
    grad_flat = rows[:, :, proj_rank:].reshape(seq_count, row_width * proj_rank)
    pre_flat = rows[:, :, :proj_rank].reshape(seq_count, row_width * proj_rank)
    lang_total = owner.shape[0]
    dp_size = lax.axis_size("dp")
    slot_count = (lang_total + dp_size - 1) // dp_size
    owned_rows = slot_count * dp_size
    lang_index = jnp.arange(lang_total, dtype=jnp.int32)
    same_owner = (owner[:, None] == owner[None, :]) & (lang_index[None, :] < lang_index[:, None])
    lang_slot = jnp.sum(same_owner.astype(jnp.int32), axis=1)
    lang_place = owner * slot_count + lang_slot
    lang_hot = (language[:, None] == lang_index[None, :]).astype(jnp.int32)
    seq_place = jnp.sum(lang_hot * lang_place[None, :], axis=1)
    slot_index = jnp.arange(owned_rows, dtype=jnp.int32).reshape(dp_size, slot_count)
    place_match = seq_place[:, None, None] == slot_index[None]
    slot_sums = jnp.sum(jnp.where(place_match[..., None], pre_flat[:, None, None, :], 0.0), axis=0)
    slot_counts = jnp.sum(place_match.astype(jnp.float32), axis=0)
    count_pad = 128
    payload = jnp.concatenate(
        [slot_sums, jnp.pad(slot_counts[:, :, None], ((0, 0), (0, 0), (0, count_pad - 1)))],
        axis=2,
    )
    gathered = jnp.sum(lax.all_to_all(payload, "dp", 0, 0, tiled=True), axis=0)
    width = pre_flat.shape[1]
    owned_means = gathered[:, :width] / jnp.maximum(gathered[:, width], 1.0)[:, None]
    return (grad_flat, owned_means)


def solution(mesh):
    return jax.shard_map(
        per_device,
        mesh=mesh,
        in_specs=(
            P("dp", None, "tensor"),
            P("dp", None, "tensor"),
            P(None, "tensor"),
            P(None, "tensor"),
            P(),
            P(),
            P("dp"),
            P("dp"),
            P(),
        ),
        out_specs=(P("dp", "tensor"), P("dp", "tensor")),
        check_vma=False,
    )
```

```python
import jax
import jax.numpy as jnp
from jax import lax
from jax.experimental import pallas as pl
from jax.sharding import PartitionSpec as P


def _project_kernel(hidden_ref, grad_ref, proj_in_ref, proj_out_ref, out_ref):
    contract = (((1,), (1,)), ((), ()))
    rank = proj_in_ref.shape[0]
    out_ref[:, :rank] = lax.dot_general(
        hidden_ref[...], proj_in_ref[...], contract, preferred_element_type=jnp.float32
    )
    out_ref[:, rank:] = lax.dot_general(
        grad_ref[...], proj_out_ref[...], contract, preferred_element_type=jnp.float32
    )


def project_both(hidden, out_grad, proj_in, proj_out, tile):
    hidden = hidden.reshape(-1, hidden.shape[-1])
    out_grad = out_grad.reshape(-1, out_grad.shape[-1])
    tokens = hidden.shape[0]
    rank = proj_in.shape[0]
    return pl.pallas_call(
        _project_kernel,
        grid=(tokens // tile,),
        in_specs=[
            pl.BlockSpec((tile, hidden.shape[1]), lambda i: (i, 0)),
            pl.BlockSpec((tile, out_grad.shape[1]), lambda i: (i, 0)),
            pl.BlockSpec(proj_in.shape, lambda i: (0, 0)),
            pl.BlockSpec(proj_out.shape, lambda i: (0, 0)),
        ],
        out_specs=pl.BlockSpec((tile, 2 * rank), lambda i: (i, 0)),
        out_shape=jax.ShapeDtypeStruct((tokens, 2 * rank), jnp.float32),
    )(hidden, out_grad, proj_in, proj_out)


def per_device(hidden, out_grad, proj_in, proj_out, left_inv, right_inv, lengths, language, owner):
    high = lax.Precision.HIGH
    seq_count = hidden.shape[0]
    seq_length = hidden.shape[1]
    proj_rank = proj_in.shape[0]
    tensor_size = lax.axis_size("tensor")
    row_width = proj_rank // tensor_size
    parts = project_both(hidden, out_grad, proj_in, proj_out, seq_count * seq_length // 2)
    tokens = seq_count * seq_length
    block = tokens // tensor_size
    chunks = parts.reshape(tensor_size, block, 2 * proj_rank)
    mine = jnp.sum(lax.all_to_all(chunks, "tensor", 0, 0, tiled=True), axis=0)
    token_at = lax.axis_index("tensor") * block + jnp.arange(block, dtype=jnp.int32)
    token_seq = token_at // seq_length
    token_pos = token_at % seq_length
    seq_index = jnp.arange(seq_count, dtype=jnp.int32)
    weight = (token_seq[None, :] == seq_index[:, None]) & (token_pos[None, :] < lengths[:, None])
    double = 2 * proj_rank
    spread = jnp.zeros((double, double), jnp.float32)
    spread = spread.at[proj_rank:, :proj_rank].set(right_inv)
    spread = spread.at[proj_rank:, proj_rank:].set(jnp.eye(proj_rank, dtype=jnp.float32))
    right_both = jnp.dot(mine, spread, precision=lax.Precision.HIGHEST)
    right_seq = right_both[:, None, :] * weight.T.astype(jnp.float32)[:, :, None]
    right_seq = right_seq.reshape(block, seq_count * double)
    grads_part = lax.dot_general(
        mine[:, :proj_rank], right_seq, (((0,), (0,)), ((), ())), precision=high
    )
    left_done = jnp.dot(left_inv, grads_part, precision=high)
    lane = jnp.arange(seq_count * double, dtype=jnp.int32) % double
    shares = jnp.where(lane[None, :] < proj_rank, left_done, grads_part)
    stacked = shares.reshape(tensor_size, row_width, seq_count * double)
    rows = jnp.sum(lax.all_to_all(stacked, "tensor", 0, 0, tiled=True), axis=0)
    rows = rows.reshape(row_width, seq_count, double).transpose(1, 0, 2)
    grad_flat = rows[:, :, proj_rank:].reshape(seq_count, row_width * proj_rank)
    pre_flat = rows[:, :, :proj_rank].reshape(seq_count, row_width * proj_rank)
    lang_total = owner.shape[0]
    dp_size = lax.axis_size("dp")
    slot_count = (lang_total + dp_size - 1) // dp_size
    owned_rows = slot_count * dp_size
    lang_index = jnp.arange(lang_total, dtype=jnp.int32)
    same_owner = (owner[:, None] == owner[None, :]) & (lang_index[None, :] < lang_index[:, None])
    lang_slot = jnp.sum(same_owner.astype(jnp.int32), axis=1)
    lang_place = owner * slot_count + lang_slot
    lang_hot = (language[:, None] == lang_index[None, :]).astype(jnp.int32)
    seq_place = jnp.sum(lang_hot * lang_place[None, :], axis=1)
    slot_index = jnp.arange(owned_rows, dtype=jnp.int32).reshape(dp_size, slot_count)
    place_match = seq_place[:, None, None] == slot_index[None]
    slot_sums = jnp.sum(jnp.where(place_match[..., None], pre_flat[:, None, None, :], 0.0), axis=0)
    slot_counts = jnp.sum(place_match.astype(jnp.float32), axis=0)
    count_pad = 128
    payload = jnp.concatenate(
        [slot_sums, jnp.pad(slot_counts[:, :, None], ((0, 0), (0, 0), (0, count_pad - 1)))],
        axis=2,
    )
    gathered = jnp.sum(lax.all_to_all(payload, "dp", 0, 0, tiled=True), axis=0)
    width = pre_flat.shape[1]
    owned_means = gathered[:, :width] / jnp.maximum(gathered[:, width], 1.0)[:, None]
    return (grad_flat, owned_means)


def solution(mesh):
    return jax.shard_map(
        per_device,
        mesh=mesh,
        in_specs=(
            P("dp", None, "tensor"),
            P("dp", None, "tensor"),
            P(None, "tensor"),
            P(None, "tensor"),
            P(),
            P(),
            P("dp"),
            P("dp"),
            P(),
        ),
        out_specs=(P("dp", "tensor"), P("dp", "tensor")),
        check_vma=False,
    )
```
